512 devices in a mesh: lon: 32 (over z, y_lo), lat: 16 (over y_hi, x, core).
Axes of the slice: x: 4, y: 4 (y_hi: 2, y_lo: 2; y = y_hi * 2 + y_lo), z: 16, core: 2. Of those that a mesh axis runs over, the one named last changes fastest.
Arguments:
- field: bfloat16 [2, 128, 128, 4096], P(None, 'lat', None, 'lon'), may hold values from -6 to 6
- weights: bfloat16 [2, 9, 128, 128], replicated, may hold values from -0.5 to 0.5
- coefs: bfloat16 [4, 128, 9, 4096], P(None, 'lat', None, 'lon'), may hold values from -2 to 2
- land_mask: int32 [2, 128, 4096], P(None, 'lat', 'lon'), may hold values 0 or 1
- fold_flag: int32 [128], replicated, may hold values from 0 to 1
Outputs:
- forward: bfloat16 [2, 128, 128, 4096], P(None, 'lat', None, 'lon')
- adjoint: bfloat16 [2, 128, 128, 4096], P(None, 'lat', None, 'lon')
The draws below stay inside these ranges and needn't reach their ends.
Inputs may be any that keep to these rules, and one draw needn't show every extreme that they name: `land_mask`: 1 marks an ocean cell, 0 land. `fold_flag`: 1 marks a channel that holds a vector component, which changes sign across the north fold.
All inputs are finite; a program needn't handle non-finite values. No bound on the sum of `land_mask` on one device may be relied on, other than what follows from the above.
Results may differ from the reference program's by a relative error of at most 0.007.
Values may be sent and summed in bfloat16 or wider, within the bound.
No kernel may reach another device: no remote copies, remote signals or barrier semaphores. Data moves between devices by JAX's collectives and lax.ppermute only.
A program may use at most 64 MiB of HBM per device.

```python
import jax
import jax.numpy as jnp
from jax import lax

C = 128
TAPS = 9
LAYERS = 2
LEV = 2
NLAT = 128
NLON = 4096


def touch_ends(values, stream_key, low, largest):
    place = [jax.random.randint(jax.random.fold_in(stream_key, axis), (), 0, length) for axis, length in enumerate(values.shape)]
    widest = values.shape.index(max(values.shape))
    next_to = place[:widest] + [(place[widest] + 1) % values.shape[widest]] + place[widest + 1:]
    return values.at[tuple(place)].set(low).at[tuple(next_to)].set(largest)


def level_of(rng, shape, split, low, largest):
    gain = 1.0
    for dim, shards_of in split:
        heights = jax.random.uniform(jax.random.fold_in(jax.random.fold_in(rng, 6), dim), (shards_of,), jnp.float32, low / len(split), largest / len(split))
        gain = gain * jnp.repeat(jnp.exp(heights), shape[dim] // shards_of).reshape((-1,) + (1,) * (len(shape) - 1 - dim))
    return gain


def normal_values(key, dims, scale, most, pieces=(), kind=jnp.bfloat16):
    factor_of = level_of(key, dims, pieces, -0.22, 0.18) if pieces else 1.0
    result = jax.random.normal(key, dims, jnp.float32) * scale * factor_of
    return jnp.minimum(jnp.maximum(result, -most), most).astype(kind)


def setup_inputs(seed: int = 0) -> dict:
    keys = jax.random.split(jax.random.key(seed), 6)
    return {
        "field": normal_values(keys[0], (LEV, NLAT, C, NLON), 1.0, 6.0, ((1, 16), (3, 32))),
        "weights": normal_values(keys[1], (LAYERS, TAPS, C, C), C ** -0.5, 0.5),
        "coefs": normal_values(keys[2], (LAYERS * LEV, NLAT, TAPS, NLON), 0.33, 2.0, ((1, 16), (3, 32))),
        "land_mask": touch_ends((jax.random.randint(keys[3], (LEV, NLAT, NLON), 0, 4) < 3).astype(jnp.int32), jax.random.fold_in(keys[3], 1), 0, 1),
        "fold_flag": touch_ends(jax.random.randint(keys[4], (C,), 0, 2), jax.random.fold_in(keys[4], 1), 0, 1).astype(jnp.int32),
    }


def extend(values, fold_flag):
    south_row = jnp.zeros_like(values[:, :1])
    top_reversed = values[:, -1:, :, ::-1]
    north_row = jnp.where(fold_flag[None, None, :, None] == 1, -top_reversed, top_reversed)
    rows_added = jnp.concatenate([south_row, values, north_row], axis=1)
    return jnp.concatenate([rows_added[..., -1:], rows_added, rows_added[..., :1]], axis=3)

def apply_layer(values, weight_set, coef_set, land_mask, fold_flag):
    extended = extend(values, fold_flag)
    accumulated = jnp.zeros(values.shape, jnp.float32)
    for tap in range(TAPS):
        step_row = tap // 3 - 1
        step_col = tap % 3 - 1
        window = extended[:, 1 + step_row:1 + step_row + NLAT, :, 1 + step_col:1 + step_col + NLON].astype(jnp.float32)
        product = jnp.einsum('oc,ljci->ljoi', weight_set[tap].astype(jnp.float32), window, precision=lax.Precision.HIGHEST)
        accumulated = accumulated + coef_set[:, :, tap, None, :].astype(jnp.float32) * product
    return accumulated * land_mask[:, :, None, :].astype(jnp.float32)

def reference(field, weights, coefs, land_mask, fold_flag):
    current = field
    for layer in range(LAYERS):
        current = apply_layer(current, weights[layer], coefs[layer * LEV:(layer + 1) * LEV], land_mask, fold_flag).astype(jnp.bfloat16)
    forward = current
    adjoint_now = forward
    for layer in reversed(range(LAYERS)):

        def linear(values, layer_index=layer):
            return apply_layer(values, weights[layer_index], coefs[layer_index * LEV:(layer_index + 1) * LEV], land_mask, fold_flag)
        _, pullback = jax.vjp(linear, jnp.zeros(field.shape, jnp.float32))
        adjoint_now = pullback(adjoint_now.astype(jnp.float32))[0].astype(jnp.bfloat16)
    return (forward, adjoint_now)
```

```python
import jax
import jax.numpy as jnp
from jax import lax
from jax.sharding import PartitionSpec as P

HALO = 4


def exchange(block, fold_sign, taps, layers, channels):
    rows = block.shape[1]
    cols = block.shape[3]
    nlon = lax.axis_size("lon")
    nlat = lax.axis_size("lat")
    to_right = [(i, (i + 1) % nlon) for i in range(nlon)]
    to_left = [((i + 1) % nlon, i) for i in range(nlon)]
    from_left = lax.ppermute(block[..., cols - HALO :], "lon", to_right)
    from_right = lax.ppermute(block[..., :HALO], "lon", to_left)
    wide = jnp.concatenate([from_left, block, from_right], axis=3)

    to_up = [(j, j + 1) for j in range(nlat - 1)]
    to_down = [(j + 1, j) for j in range(nlat - 1)]
    below = lax.ppermute(wide[:, rows - HALO :], "lat", to_up)
    above = lax.ppermute(wide[:, :HALO], "lat", to_down)
    top = nlat - 1
    mirror_pairs = [(b * nlat + top, (nlon - 1 - b) * nlat + top) for b in range(nlon)]
    mirrored = lax.ppermute(wide[:, rows - HALO :], ("lon", "lat"), mirror_pairs)
    mirrored = mirrored[:, ::-1, :, ::-1]
    field_part = mirrored[:, :, :channels] * fold_sign[None, None, :, None]
    coef_part = mirrored[:, :, channels : channels + layers * taps]
    coef_part = coef_part.reshape(
        coef_part.shape[0], coef_part.shape[1], layers, taps, coef_part.shape[3]
    )[:, :, :, ::-1].reshape(coef_part.shape)
    rest = mirrored[:, :, channels + layers * taps :]
    mirrored = jnp.concatenate([field_part, coef_part, rest], axis=2)
    is_top = lax.axis_index("lat") == top
    above = jnp.where(is_top, mirrored, above)
    return jnp.concatenate([below, wide, above], axis=1)


def tap_offsets(tap):
    return tap // 3 - 1, tap % 3 - 1


def forward_layer(x, first_row, weights_low, weights_high, coef, mask, split):
    n_rows = x.shape[1] - 2
    n_cols = x.shape[3] - 2
    out_first = first_row + 1
    cut = min(max(split - out_first, 0), n_rows)
    parts = []
    for lo, hi, weight_set in ((0, cut, weights_low), (cut, n_rows, weights_high)):
        if hi <= lo:
            continue
        acc = None
        for tap in range(weight_set.shape[0]):
            dj, di = tap_offsets(tap)
            window = x[:, 1 + lo + dj : 1 + hi + dj, :, 1 + di : 1 + di + n_cols]
            product = jnp.einsum(
                "oc,ljci->ljoi", weight_set[tap], window, preferred_element_type=jnp.float32
            )
            term = coef[:, 1 + lo : 1 + hi, tap, None, 1 : 1 + n_cols].astype(jnp.float32) * product
            acc = term if acc is None else acc + term
        parts.append(acc)
    acc = jnp.concatenate(parts, axis=1) if len(parts) > 1 else parts[0]
    return (acc * mask[:, 1 : 1 + n_rows, None, 1 : 1 + n_cols]).astype(jnp.bfloat16)


def adjoint_layer(g, first_row, weights_low, weights_high, coef, mask, split):
    n_src_rows = g.shape[1]
    n_rows = n_src_rows - 2
    n_cols = g.shape[3] - 2
    masked = g * mask[:, :, None, :]
    cut = min(max(split - first_row, 0), n_src_rows)
    acc = None
    for tap in range(weights_low.shape[0]):
        dj, di = tap_offsets(tap)
        pieces = []
        for lo, hi, weight_set in ((0, cut, weights_low), (cut, n_src_rows, weights_high)):
            if hi <= lo:
                continue
            pieces.append(
                jnp.einsum(
                    "oc,ljoi->ljci",
                    weight_set[tap],
                    masked[:, lo:hi],
                    preferred_element_type=jnp.float32,
                )
            )
        product = jnp.concatenate(pieces, axis=1) if len(pieces) > 1 else pieces[0]
        scaled = coef[:, :, tap, None, :].astype(jnp.float32) * product
        term = scaled[:, 1 - dj : 1 - dj + n_rows, :, 1 - di : 1 - di + n_cols]
        acc = term if acc is None else acc + term
    return acc.astype(jnp.bfloat16)


def local(field, weights, coefs, land_mask, fold_flag):
    layers, taps = weights.shape[0], weights.shape[1]
    levels, rows, channels, cols = field.shape
    fold_sign = jnp.where(fold_flag == 1, -1.0, 1.0).astype(jnp.bfloat16)
    coef_stack = (
        coefs.reshape(layers, levels, rows, taps, cols)
        .transpose(1, 2, 0, 3, 4)
        .reshape(levels, rows, layers * taps, cols)
    )
    mask_stack = land_mask.astype(jnp.bfloat16)[:, :, None, :]
    block = jnp.concatenate([field, coef_stack, mask_stack], axis=2)
    ext = exchange(block, fold_sign, taps, layers, channels)
    x = ext[:, :, :channels]
    coef_ext = ext[:, :, channels : channels + layers * taps]
    mask_ext = ext[:, :, channels + layers * taps].astype(jnp.float32)

    is_top = lax.axis_index("lat") == lax.axis_size("lat") - 1
    flipped = weights[:, ::-1] * fold_sign[None, None, :, None] * fold_sign[None, None, None, :]
    weights_high = jnp.where(is_top, flipped, weights)

    split = rows
    first = -HALO
    current = x
    for layer in range(layers):
        shrink = layer
        coef_l = coef_ext[:, shrink : ext.shape[1] - shrink, layer * taps : (layer + 1) * taps]
        coef_l = coef_l[..., shrink : ext.shape[3] - shrink]
        mask_l = mask_ext[:, shrink : ext.shape[1] - shrink, shrink : ext.shape[3] - shrink]
        current = forward_layer(
            current, first, weights[layer], weights_high[layer], coef_l, mask_l, split
        )
        first += 1
    forward = current[:, HALO - layers : HALO - layers + rows, :, HALO - layers : HALO - layers + cols]
    adjoint_now = current
    for layer in reversed(range(layers)):
        shrink = HALO - (adjoint_now.shape[1] - rows) // 2
        coef_l = coef_ext[:, shrink : ext.shape[1] - shrink, layer * taps : (layer + 1) * taps]
        coef_l = coef_l[..., shrink : ext.shape[3] - shrink]
        mask_l = mask_ext[:, shrink : ext.shape[1] - shrink, shrink : ext.shape[3] - shrink]
        adjoint_now = adjoint_layer(
            adjoint_now, first, weights[layer], weights_high[layer], coef_l, mask_l, split
        )
        first += 1
    return (forward, adjoint_now)


def solution(mesh):
    return jax.shard_map(
        local,
        mesh=mesh,
        in_specs=(
            P(None, "lat", None, "lon"),
            P(),
            P(None, "lat", None, "lon"),
            P(None, "lat", "lon"),
            P(),
        ),
        out_specs=(P(None, "lat", None, "lon"), P(None, "lat", None, "lon")),
        check_vma=False,
    )
```

```python
import functools

import jax
import jax.numpy as jnp
from jax import lax
from jax.experimental import pallas as pl
from jax.experimental.pallas import tpu as pltpu
from jax.sharding import PartitionSpec as P

HALO = 4
PAD = 8


def exchange(block, fold_sign, taps, layers, channels):
    rows = block.shape[1]
    cols = block.shape[2]
    nlon = lax.axis_size("lon")
    nlat = lax.axis_size("lat")
    to_right = [(i, (i + 1) % nlon) for i in range(nlon)]
    to_left = [((i + 1) % nlon, i) for i in range(nlon)]
    from_left = lax.ppermute(block[:, :, cols - HALO :], "lon", to_right)
    from_right = lax.ppermute(block[:, :, :HALO], "lon", to_left)
    wide = jnp.concatenate([from_left, block, from_right], axis=2)

    to_up = [(j, j + 1) for j in range(nlat - 1)]
    to_down = [(j + 1, j) for j in range(nlat - 1)]
    below = lax.ppermute(wide[:, rows - HALO :], "lat", to_up)
    above = lax.ppermute(wide[:, :HALO], "lat", to_down)
    top = nlat - 1
    mirror_pairs = [(b * nlat + top, (nlon - 1 - b) * nlat + top) for b in range(nlon)]
    mirrored = lax.ppermute(wide[:, rows - HALO :], ("lon", "lat"), mirror_pairs)
    mirrored = mirrored[:, ::-1, ::-1]
    field_part = mirrored[..., :channels] * fold_sign
    coef_part = mirrored[..., channels : channels + layers * taps]
    coef_part = coef_part.reshape(coef_part.shape[:3] + (layers, taps))[..., ::-1].reshape(
        coef_part.shape
    )
    rest = mirrored[..., channels + layers * taps :]
    mirrored = jnp.concatenate([field_part, coef_part, rest], axis=3)
    is_top = lax.axis_index("lat") == top
    above = jnp.where(is_top, mirrored, above)
    return jnp.concatenate([below, wide, above], axis=1)


def stencil_kernel(x_ref, aux_ref, w_ref, o_ref, *, row_lo, row_hi, coef_lane, mask_lane, split, adjoint):
    levels = x_ref.shape[0]
    out_cols = x_ref.shape[2] - 2 * PAD
    chans = x_ref.shape[3]
    n = row_hi - row_lo
    o_ref[...] = jnp.zeros(o_ref.shape, o_ref.dtype)

    def body(idx, carry):
        lev = idx // n
        j = row_lo + idx % n
        acc = jnp.zeros((out_cols, chans), jnp.float32)
        for tap in range(w_ref.shape[1]):
            dj, di = tap // 3 - 1, tap % 3 - 1
            if adjoint:
                src = j - dj
                col = PAD - di
                xin = x_ref[lev, src, pl.ds(col, out_cols), :]
                xin = xin * aux_ref[lev, src, pl.ds(col, out_cols), pl.ds(mask_lane, 1)]
                cf = aux_ref[lev, src, pl.ds(col, out_cols), pl.ds(coef_lane + tap, 1)]
                sel = (src >= split).astype(jnp.int32)
            else:
                src = j + dj
                col = PAD + di
                xin = x_ref[lev, src, pl.ds(col, out_cols), :]
                cf = aux_ref[lev, j, pl.ds(PAD, out_cols), pl.ds(coef_lane + tap, 1)]
                sel = (j >= split).astype(jnp.int32)
            prod = jnp.dot(
                xin.astype(jnp.bfloat16), w_ref[sel, tap], preferred_element_type=jnp.float32
            )
            acc = acc + cf * prod
        if not adjoint:
            acc = acc * aux_ref[lev, j, pl.ds(PAD, out_cols), pl.ds(mask_lane, 1)]
        o_ref[lev, j, pl.ds(PAD, out_cols), :] = acc.astype(jnp.bfloat16).astype(jnp.float32)
        return carry

    lax.fori_loop(0, levels * n, body, 0)


def stencil(x, aux, w, row_lo, row_hi, coef_lane, mask_lane, split, adjoint):
    kernel = functools.partial(
        stencil_kernel,
        row_lo=row_lo,
        row_hi=row_hi,
        coef_lane=coef_lane,
        mask_lane=mask_lane,
        split=split,
        adjoint=adjoint,
    )
    levels, _, width, chans = x.shape
    rows_done = row_hi - row_lo
    flops = 2 * levels * rows_done * (width - 2 * PAD) * chans * chans * w.shape[1]
    return pl.pallas_call(
        kernel,
        out_shape=jax.ShapeDtypeStruct(x.shape, jnp.float32),
        in_specs=[pl.BlockSpec(memory_space=pltpu.VMEM)] * 3,
        out_specs=pl.BlockSpec(memory_space=pltpu.VMEM),
        cost_estimate=pl.CostEstimate(
            flops=flops, bytes_accessed=2 * x.size * 4 + aux.size * 4, transcendentals=0
        ),
    )(x, aux, w)


def local(field, weights, coefs, land_mask, fold_flag):
    layers, taps = weights.shape[0], weights.shape[1]
    levels, rows, channels, cols = field.shape
    fold_sign = jnp.where(fold_flag == 1, -1.0, 1.0).astype(jnp.bfloat16)
    coef_stack = (
        coefs.reshape(layers, levels, rows, taps, cols)
        .transpose(1, 2, 4, 0, 3)
        .reshape(levels, rows, cols, layers * taps)
    )
    mask_stack = land_mask.astype(jnp.bfloat16)[..., None]
    block = jnp.concatenate([field.transpose(0, 1, 3, 2), coef_stack, mask_stack], axis=3)
    ext = exchange(block, fold_sign, taps, layers, channels)
    ext = jnp.pad(ext, ((0, 0), (0, 0), (PAD, PAD), (0, 0))).astype(jnp.float32)
    x = ext[..., :channels]
    aux = ext[..., channels:]
    mask_lane = layers * taps

    is_top = lax.axis_index("lat") == lax.axis_size("lat") - 1
    flipped = weights[:, ::-1] * fold_sign[None, None, :, None] * fold_sign[None, None, None, :]
    weights_high = jnp.where(is_top, flipped, weights)
    both = jnp.stack([weights, weights_high], axis=1)
    forward_w = both.transpose(0, 1, 2, 4, 3)

    split = HALO + rows
    total_rows = ext.shape[1]
    current = x
    for layer in range(layers):
        current = stencil(
            current,
            aux,
            forward_w[layer],
            layer + 1,
            total_rows - layer - 1,
            layer * taps,
            mask_lane,
            split,
            False,
        )
    forward_rows = current[:, HALO : HALO + rows, PAD + HALO : PAD + HALO + cols]
    forward = forward_rows.transpose(0, 1, 3, 2).astype(jnp.bfloat16)
    adjoint_now = current
    depth = layers
    for layer in reversed(range(layers)):
        depth += 1
        adjoint_now = stencil(
            adjoint_now,
            aux,
            both[layer],
            depth,
            total_rows - depth,
            layer * taps,
            mask_lane,
            split,
            True,
        )
    adjoint_rows = adjoint_now[:, HALO : HALO + rows, PAD + HALO : PAD + HALO + cols]
    return (forward, adjoint_rows.transpose(0, 1, 3, 2).astype(jnp.bfloat16))


def solution(mesh):
    return jax.shard_map(
        local,
        mesh=mesh,
        in_specs=(
            P(None, "lat", None, "lon"),
            P(),
            P(None, "lat", None, "lon"),
            P(None, "lat", "lon"),
            P(),
        ),
        out_specs=(P(None, "lat", None, "lon"), P(None, "lat", None, "lon")),
        check_vma=False,
    )
```

```python
import functools

import jax
import jax.numpy as jnp
from jax import lax
from jax.experimental import pallas as pl
from jax.experimental.pallas import tpu as pltpu
from jax.sharding import PartitionSpec as P

HALO = 4
PAD = 8


def exchange(block, fold_sign, taps, layers, channels):
    rows = block.shape[1]
    cols = block.shape[2]
    nlon = lax.axis_size("lon")
    nlat = lax.axis_size("lat")
    to_right = [(i, (i + 1) % nlon) for i in range(nlon)]
    to_left = [((i + 1) % nlon, i) for i in range(nlon)]
    from_left = lax.ppermute(block[:, :, cols - HALO :], "lon", to_right)
    from_right = lax.ppermute(block[:, :, :HALO], "lon", to_left)
    wide = jnp.concatenate([from_left, block, from_right], axis=2)

    to_up = [(j, j + 1) for j in range(nlat - 1)]
    to_down = [(j + 1, j) for j in range(nlat - 1)]
    below = lax.ppermute(wide[:, rows - HALO :], "lat", to_up)
    above = lax.ppermute(wide[:, :HALO], "lat", to_down)
    top = nlat - 1
    mirror_pairs = [(b * nlat + top, (nlon - 1 - b) * nlat + top) for b in range(nlon)]
    mirrored = lax.ppermute(wide[:, rows - HALO :], ("lon", "lat"), mirror_pairs)
    mirrored = mirrored[:, ::-1, ::-1]
    field_part = mirrored[..., :channels] * fold_sign
    coef_part = mirrored[..., channels : channels + layers * taps]
    coef_part = coef_part.reshape(coef_part.shape[:3] + (layers, taps))[..., ::-1].reshape(
        coef_part.shape
    )
    rest = mirrored[..., channels + layers * taps :]
    mirrored = jnp.concatenate([field_part, coef_part, rest], axis=3)
    is_top = lax.axis_index("lat") == top
    above = jnp.where(is_top, mirrored, above)
    return jnp.concatenate([below, wide, above], axis=1)


def stencil_kernel(x_ref, aux_ref, w_ref, o_ref, acc_ref, *, row_lo, row_hi, coef_lane, mask_lane, split, adjoint):
    levels = x_ref.shape[0]
    out_cols = x_ref.shape[2] - 2 * PAD
    chans = x_ref.shape[3]
    o_ref[...] = jnp.zeros(o_ref.shape, o_ref.dtype)

    def level_body(lev, carry):
        acc_ref[...] = jnp.zeros(acc_ref.shape, acc_ref.dtype)
        for tap in range(w_ref.shape[1]):
            dj, di = tap // 3 - 1, tap % 3 - 1
            step = -dj if adjoint else dj
            col = PAD - di if adjoint else PAD + di
            if adjoint:
                groups = ((row_lo, min(row_hi, split + dj), 0), (max(row_lo, split + dj), row_hi, 1))
            else:
                groups = ((row_lo, min(row_hi, split), 0), (max(row_lo, split), row_hi, 1))
            for lo, hi, sel in groups:
                if hi <= lo:
                    continue
                count = hi - lo
                src = slice(lo + step, hi + step)
                xin = x_ref[lev, src, pl.ds(col, out_cols), :].reshape(count * out_cols, chans)
                if adjoint:
                    mask_col = aux_ref[lev, src, pl.ds(col, out_cols), pl.ds(mask_lane, 1)]
                    xin = xin * mask_col.reshape(count * out_cols, 1)
                    cf = aux_ref[lev, src, pl.ds(col, out_cols), pl.ds(coef_lane + tap, 1)]
                    prod = jnp.dot(
                        xin.astype(jnp.bfloat16), w_ref[sel, tap], preferred_element_type=jnp.float32
                    )
                else:
                    cf = aux_ref[lev, lo:hi, pl.ds(PAD, out_cols), pl.ds(coef_lane + tap, 1)]
                    prod = lax.dot_general(
                        xin.astype(jnp.bfloat16),
                        w_ref[sel, tap],
                        (((1,), (1,)), ((), ())),
                        preferred_element_type=jnp.float32,
                    )
                term = cf.reshape(count * out_cols, 1) * prod
                acc_ref[lo:hi] += term.reshape(count, out_cols, chans)
        result = acc_ref[row_lo:row_hi]
        if not adjoint:
            result = result * aux_ref[lev, row_lo:row_hi, pl.ds(PAD, out_cols), pl.ds(mask_lane, 1)]
        o_ref[lev, row_lo:row_hi, pl.ds(PAD, out_cols), :] = result.astype(jnp.bfloat16).astype(
            jnp.float32
        )
        return carry

    lax.fori_loop(0, levels, level_body, 0)


def stencil(x, aux, w, row_lo, row_hi, coef_lane, mask_lane, split, adjoint):
    kernel = functools.partial(
        stencil_kernel,
        row_lo=row_lo,
        row_hi=row_hi,
        coef_lane=coef_lane,
        mask_lane=mask_lane,
        split=split,
        adjoint=adjoint,
    )
    levels, total_rows, width, chans = x.shape
    rows_done = row_hi - row_lo
    flops = 2 * levels * rows_done * (width - 2 * PAD) * chans * chans * w.shape[1]
    return pl.pallas_call(
        kernel,
        out_shape=jax.ShapeDtypeStruct(x.shape, jnp.float32),
        in_specs=[pl.BlockSpec(memory_space=pltpu.VMEM)] * 3,
        out_specs=pl.BlockSpec(memory_space=pltpu.VMEM),
        scratch_shapes=[pltpu.VMEM((total_rows, width - 2 * PAD, chans), jnp.float32)],
        cost_estimate=pl.CostEstimate(
            flops=flops, bytes_accessed=2 * x.size * 4 + aux.size * 4, transcendentals=0
        ),
    )(x, aux, w)


def local(field, weights, coefs, land_mask, fold_flag):
    layers, taps = weights.shape[0], weights.shape[1]
    levels, rows, channels, cols = field.shape
    fold_sign = jnp.where(fold_flag == 1, -1.0, 1.0).astype(jnp.bfloat16)
    coef_stack = (
        coefs.reshape(layers, levels, rows, taps, cols)
        .transpose(1, 2, 4, 0, 3)
        .reshape(levels, rows, cols, layers * taps)
    )
    mask_stack = land_mask.astype(jnp.bfloat16)[..., None]
    block = jnp.concatenate([field.transpose(0, 1, 3, 2), coef_stack, mask_stack], axis=3)
    ext = exchange(block, fold_sign, taps, layers, channels)
    ext = jnp.pad(ext, ((0, 0), (0, 0), (PAD, PAD), (0, 0))).astype(jnp.float32)
    x = ext[..., :channels]
    aux = ext[..., channels:]
    mask_lane = layers * taps

    is_top = lax.axis_index("lat") == lax.axis_size("lat") - 1
    flipped = weights[:, ::-1] * fold_sign[None, None, :, None] * fold_sign[None, None, None, :]
    weights_high = jnp.where(is_top, flipped, weights)
    both = jnp.stack([weights, weights_high], axis=1)

    split = HALO + rows
    total_rows = ext.shape[1]
    current = x
    for layer in range(layers):
        current = stencil(
            current,
            aux,
            both[layer],
            layer + 1,
            total_rows - layer - 1,
            layer * taps,
            mask_lane,
            split,
            False,
        )
    forward_rows = current[:, HALO : HALO + rows, PAD + HALO : PAD + HALO + cols]
    forward = forward_rows.transpose(0, 1, 3, 2).astype(jnp.bfloat16)
    adjoint_now = current
    depth = layers
    for layer in reversed(range(layers)):
        depth += 1
        adjoint_now = stencil(
            adjoint_now,
            aux,
            both[layer],
            depth,
            total_rows - depth,
            layer * taps,
            mask_lane,
            split,
            True,
        )
    adjoint_rows = adjoint_now[:, HALO : HALO + rows, PAD + HALO : PAD + HALO + cols]
    return (forward, adjoint_rows.transpose(0, 1, 3, 2).astype(jnp.bfloat16))


def solution(mesh):
    return jax.shard_map(
        local,
        mesh=mesh,
        in_specs=(
            P(None, "lat", None, "lon"),
            P(),
            P(None, "lat", None, "lon"),
            P(None, "lat", "lon"),
            P(),
        ),
        out_specs=(P(None, "lat", None, "lon"), P(None, "lat", None, "lon")),
        check_vma=False,
    )
```

```python
import functools

import jax
import jax.numpy as jnp
from jax import lax
from jax.experimental import pallas as pl
from jax.experimental.pallas import tpu as pltpu
from jax.sharding import PartitionSpec as P

HALO = 4
PAD = 8


def exchange(block, fold_sign, taps, layers, channels):
    rows = block.shape[1]
    cols = block.shape[2]
    nlon = lax.axis_size("lon")
    nlat = lax.axis_size("lat")
    to_right = [(i, (i + 1) % nlon) for i in range(nlon)]
    to_left = [((i + 1) % nlon, i) for i in range(nlon)]
    from_left = lax.ppermute(block[:, :, cols - HALO :], "lon", to_right)
    from_right = lax.ppermute(block[:, :, :HALO], "lon", to_left)

    top = nlat - 1
    top_rows = block[:, rows - HALO :]

    def across(piece, shift):
        pairs = [(b * nlat + top, ((shift - b) % nlon) * nlat + top) for b in range(nlon)]
        return lax.ppermute(piece, ("lon", "lat"), pairs)

    mirror_low = across(top_rows[:, :, cols - HALO :], nlon - 2)
    mirror_mid = across(top_rows, nlon - 1)
    mirror_high = across(top_rows[:, :, :HALO], nlon)
    mirrored = jnp.concatenate([mirror_low, mirror_mid, mirror_high], axis=2)
    wide = jnp.concatenate([from_left, block, from_right], axis=2)

    to_up = [(j, j + 1) for j in range(nlat - 1)]
    to_down = [(j + 1, j) for j in range(nlat - 1)]
    below = lax.ppermute(wide[:, rows - HALO :], "lat", to_up)
    above = lax.ppermute(wide[:, :HALO], "lat", to_down)
    mirrored = mirrored[:, ::-1, ::-1]
    field_part = mirrored[..., :channels] * fold_sign
    coef_part = mirrored[..., channels : channels + layers * taps]
    coef_part = coef_part.reshape(coef_part.shape[:3] + (layers, taps))[..., ::-1].reshape(
        coef_part.shape
    )
    rest = mirrored[..., channels + layers * taps :]
    mirrored = jnp.concatenate([field_part, coef_part, rest], axis=3)
    is_top = lax.axis_index("lat") == top
    above = jnp.where(is_top, mirrored, above)
    return jnp.concatenate([below, wide, above], axis=1)


def stencil_kernel(x_ref, aux_ref, w_ref, o_ref, acc_ref, *, row_lo, row_hi, coef_lane, mask_lane, split, adjoint):
    levels = x_ref.shape[0]
    out_cols = x_ref.shape[2] - 2 * PAD
    chans = x_ref.shape[3]
    o_ref[...] = jnp.zeros(o_ref.shape, o_ref.dtype)

    def level_body(lev, carry):
        acc_ref[...] = jnp.zeros(acc_ref.shape, acc_ref.dtype)
        for tap in range(w_ref.shape[1]):
            dj, di = tap // 3 - 1, tap % 3 - 1
            step = -dj if adjoint else dj
            col = PAD - di if adjoint else PAD + di
            if adjoint:
                groups = ((row_lo, min(row_hi, split + dj), 0), (max(row_lo, split + dj), row_hi, 1))
            else:
                groups = ((row_lo, min(row_hi, split), 0), (max(row_lo, split), row_hi, 1))
            for lo, hi, sel in groups:
                if hi <= lo:
                    continue
                count = hi - lo
                src = slice(lo + step, hi + step)
                xin = x_ref[lev, src, pl.ds(col, out_cols), :].reshape(count * out_cols, chans)
                if adjoint:
                    mask_col = aux_ref[lev, src, pl.ds(col, out_cols), pl.ds(mask_lane, 1)]
                    xin = xin * mask_col.reshape(count * out_cols, 1)
                    cf = aux_ref[lev, src, pl.ds(col, out_cols), pl.ds(coef_lane + tap, 1)]
                    prod = jnp.dot(
                        xin.astype(jnp.bfloat16), w_ref[sel, tap], preferred_element_type=jnp.float32
                    )
                else:
                    cf = aux_ref[lev, lo:hi, pl.ds(PAD, out_cols), pl.ds(coef_lane + tap, 1)]
                    prod = lax.dot_general(
                        xin.astype(jnp.bfloat16),
                        w_ref[sel, tap],
                        (((1,), (1,)), ((), ())),
                        preferred_element_type=jnp.float32,
                    )
                term = cf.reshape(count * out_cols, 1) * prod
                acc_ref[lo:hi] += term.reshape(count, out_cols, chans)
        result = acc_ref[row_lo:row_hi]
        if not adjoint:
            result = result * aux_ref[lev, row_lo:row_hi, pl.ds(PAD, out_cols), pl.ds(mask_lane, 1)]
        o_ref[lev, row_lo:row_hi, pl.ds(PAD, out_cols), :] = result.astype(jnp.bfloat16).astype(
            jnp.float32
        )
        return carry

    lax.fori_loop(0, levels, level_body, 0)


def stencil(x, aux, w, row_lo, row_hi, coef_lane, mask_lane, split, adjoint):
    kernel = functools.partial(
        stencil_kernel,
        row_lo=row_lo,
        row_hi=row_hi,
        coef_lane=coef_lane,
        mask_lane=mask_lane,
        split=split,
        adjoint=adjoint,
    )
    levels, total_rows, width, chans = x.shape
    rows_done = row_hi - row_lo
    flops = 2 * levels * rows_done * (width - 2 * PAD) * chans * chans * w.shape[1]
    return pl.pallas_call(
        kernel,
        out_shape=jax.ShapeDtypeStruct(x.shape, jnp.float32),
        in_specs=[pl.BlockSpec(memory_space=pltpu.VMEM)] * 3,
        out_specs=pl.BlockSpec(memory_space=pltpu.VMEM),
        scratch_shapes=[pltpu.VMEM((total_rows, width - 2 * PAD, chans), jnp.float32)],
        cost_estimate=pl.CostEstimate(
            flops=flops, bytes_accessed=2 * x.size * 4 + aux.size * 4, transcendentals=0
        ),
    )(x, aux, w)


def local(field, weights, coefs, land_mask, fold_flag):
    layers, taps = weights.shape[0], weights.shape[1]
    levels, rows, channels, cols = field.shape
    fold_sign = jnp.where(fold_flag == 1, -1.0, 1.0).astype(jnp.bfloat16)
    coef_stack = (
        coefs.reshape(layers, levels, rows, taps, cols)
        .transpose(1, 2, 4, 0, 3)
        .reshape(levels, rows, cols, layers * taps)
    )
    mask_stack = land_mask.astype(jnp.bfloat16)[..., None]
    block = jnp.concatenate([field.transpose(0, 1, 3, 2), coef_stack, mask_stack], axis=3)
    ext = exchange(block, fold_sign, taps, layers, channels)
    ext = jnp.pad(ext, ((0, 0), (0, 0), (PAD, PAD), (0, 0))).astype(jnp.float32)
    x = ext[..., :channels]
    aux = ext[..., channels:]
    mask_lane = layers * taps

    is_top = lax.axis_index("lat") == lax.axis_size("lat") - 1
    flipped = weights[:, ::-1] * fold_sign[None, None, :, None] * fold_sign[None, None, None, :]
    weights_high = jnp.where(is_top, flipped, weights)
    both = jnp.stack([weights, weights_high], axis=1)

    split = HALO + rows
    total_rows = ext.shape[1]
    current = x
    for layer in range(layers):
        current = stencil(
            current,
            aux,
            both[layer],
            layer + 1,
            total_rows - layer - 1,
            layer * taps,
            mask_lane,
            split,
            False,
        )
    forward_rows = current[:, HALO : HALO + rows, PAD + HALO : PAD + HALO + cols]
    forward = forward_rows.transpose(0, 1, 3, 2).astype(jnp.bfloat16)
    adjoint_now = current
    depth = layers
    for layer in reversed(range(layers)):
        depth += 1
        adjoint_now = stencil(
            adjoint_now,
            aux,
            both[layer],
            depth,
            total_rows - depth,
            layer * taps,
            mask_lane,
            split,
            True,
        )
    adjoint_rows = adjoint_now[:, HALO : HALO + rows, PAD + HALO : PAD + HALO + cols]
    return (forward, adjoint_rows.transpose(0, 1, 3, 2).astype(jnp.bfloat16))


def solution(mesh):
    return jax.shard_map(
        local,
        mesh=mesh,
        in_specs=(
            P(None, "lat", None, "lon"),
            P(),
            P(None, "lat", None, "lon"),
            P(None, "lat", "lon"),
            P(),
        ),
        out_specs=(P(None, "lat", None, "lon"), P(None, "lat", None, "lon")),
        check_vma=False,
    )
```

```python
import functools

import jax
import jax.numpy as jnp
from jax import lax
from jax.experimental import pallas as pl
from jax.experimental.pallas import tpu as pltpu
from jax.sharding import PartitionSpec as P

HALO = 4
PAD = 8


def exchange(block, block_in, fold_sign, taps, layers, channels):
    rows = block.shape[1]
    cols = block.shape[2]
    nlon = lax.axis_size("lon")
    nlat = lax.axis_size("lat")
    to_right = [(i, (i + 1) % nlon) for i in range(nlon)]
    to_left = [((i + 1) % nlon, i) for i in range(nlon)]
    from_left = lax.ppermute(block[:, :, cols - HALO :], "lon", to_right)
    from_right = lax.ppermute(block[:, :, :HALO], "lon", to_left)

    top = nlat - 1
    top_rows = block[:, rows - HALO :]

    def across(piece, shift):
        pairs = [(b * nlat + top, ((shift - b) % nlon) * nlat + top) for b in range(nlon)]
        return lax.ppermute(piece, ("lon", "lat"), pairs)

    mirror_low = across(top_rows[:, :, cols - HALO :], nlon - 2)
    mirror_mid = across(block_in[:, rows - HALO :], nlon - 1).transpose(0, 1, 3, 2)
    mirror_high = across(top_rows[:, :, :HALO], nlon)
    mirrored = jnp.concatenate([mirror_low, mirror_mid, mirror_high], axis=2)
    wide = jnp.concatenate([from_left, block, from_right], axis=2)

    to_up = [(j, j + 1) for j in range(nlat - 1)]
    to_down = [(j + 1, j) for j in range(nlat - 1)]
    below = lax.ppermute(wide[:, rows - HALO :], "lat", to_up)
    above = lax.ppermute(wide[:, :HALO], "lat", to_down)
    mirrored = mirrored[:, ::-1, ::-1]
    field_part = mirrored[..., :channels] * fold_sign
    coef_part = mirrored[..., channels : channels + layers * taps]
    coef_part = coef_part.reshape(coef_part.shape[:3] + (layers, taps))[..., ::-1].reshape(
        coef_part.shape
    )
    rest = mirrored[..., channels + layers * taps :]
    mirrored = jnp.concatenate([field_part, coef_part, rest], axis=3)
    is_top = lax.axis_index("lat") == top
    above = jnp.where(is_top, mirrored, above)
    return jnp.concatenate([below, wide, above], axis=1)


def apply_layer(x_ref, aux_ref, w_ref, o_ref, acc_ref, lev, row_lo, row_hi, coef_lane, mask_lane, split, adjoint, mg_ref=None):
    out_cols = acc_ref.shape[1]
    chans = acc_ref.shape[2]
    acc_ref[...] = jnp.zeros(acc_ref.shape, acc_ref.dtype)
    if adjoint:
        src_rows = slice(row_lo - 1, row_hi + 1)
        mg_ref[src_rows] = x_ref[lev, src_rows] * aux_ref[lev, src_rows, :, pl.ds(mask_lane, 1)]
    for tap in range(w_ref.shape[1]):
        dj, di = tap // 3 - 1, tap % 3 - 1
        step = -dj if adjoint else dj
        col = PAD - di if adjoint else PAD + di
        if adjoint:
            groups = ((row_lo, min(row_hi, split + dj), 0), (max(row_lo, split + dj), row_hi, 1))
        else:
            groups = ((row_lo, min(row_hi, split), 0), (max(row_lo, split), row_hi, 1))
        for lo, hi, sel in groups:
            if hi <= lo:
                continue
            count = hi - lo
            src = slice(lo + step, hi + step)
            if adjoint:
                xin = mg_ref[src, pl.ds(col, out_cols), :].reshape(count * out_cols, chans)
                cf = aux_ref[lev, src, pl.ds(col, out_cols), pl.ds(coef_lane + tap, 1)]
                prod = jnp.dot(
                    xin.astype(jnp.bfloat16), w_ref[sel, tap], preferred_element_type=jnp.float32
                )
            else:
                xin = x_ref[lev, src, pl.ds(col, out_cols), :].reshape(count * out_cols, chans)
                cf = aux_ref[lev, lo:hi, pl.ds(PAD, out_cols), pl.ds(coef_lane + tap, 1)]
                prod = lax.dot_general(
                    xin.astype(jnp.bfloat16),
                    w_ref[sel, tap],
                    (((1,), (1,)), ((), ())),
                    preferred_element_type=jnp.float32,
                )
            term = cf.reshape(count * out_cols, 1) * prod
            acc_ref[lo:hi] += term.reshape(count, out_cols, chans)
    result = acc_ref[row_lo:row_hi]
    if not adjoint:
        result = result * aux_ref[lev, row_lo:row_hi, pl.ds(PAD, out_cols), pl.ds(mask_lane, 1)]
    o_ref[lev, row_lo:row_hi, pl.ds(PAD, out_cols), :] = result.astype(jnp.bfloat16).astype(jnp.float32)


def model_kernel(blk_ref, w_ref, fwd_ref, adj_ref, ext_ref, aux_ref, x1_ref, x2_ref, g1_ref, acc_ref, mg_ref, *, rows, cols, layers, taps, split):
    levels, total_rows = ext_ref.shape[0], ext_ref.shape[1]
    chans = ext_ref.shape[3]
    data_cols = blk_ref.shape[2]
    mask_lane = layers * taps
    for buf in (ext_ref, aux_ref, x1_ref, x2_ref, g1_ref):
        buf[...] = jnp.zeros(buf.shape, buf.dtype)
    for lev in range(levels):
        for j in range(total_rows):
            piece = blk_ref[lev, j].astype(jnp.float32)
            ext_ref[lev, j, pl.ds(PAD, data_cols), :] = piece[:, :chans]
            aux_ref[lev, j, pl.ds(PAD, data_cols), :] = piece[:, chans:]

    def store_transposed(out_ref, src_ref, lev):
        for r in range(rows):
            tile = src_ref[lev, HALO + r, pl.ds(PAD + HALO, cols), :]
            out_ref[lev, r] = jnp.transpose(tile).astype(out_ref.dtype)

    def level_body(lev, carry):
        apply_layer(ext_ref, aux_ref, w_ref.at[0], x1_ref, acc_ref, lev, 1, total_rows - 1, 0, mask_lane, split, False)
        apply_layer(x1_ref, aux_ref, w_ref.at[1], x2_ref, acc_ref, lev, 2, total_rows - 2, taps, mask_lane, split, False)
        store_transposed(fwd_ref, x2_ref, lev)
        apply_layer(x2_ref, aux_ref, w_ref.at[1], g1_ref, acc_ref, lev, 3, total_rows - 3, taps, mask_lane, split, True, mg_ref)
        apply_layer(g1_ref, aux_ref, w_ref.at[0], x1_ref, acc_ref, lev, 4, total_rows - 4, 0, mask_lane, split, True, mg_ref)
        store_transposed(adj_ref, x1_ref, lev)
        return carry

    lax.fori_loop(0, levels, level_body, 0)


def run_model(blk, both, rows, cols, layers, taps, split):
    levels, total_rows, data_cols, lanes = blk.shape
    chans = both.shape[-1]
    width = data_cols + 2 * PAD
    kernel = functools.partial(
        model_kernel, rows=rows, cols=cols, layers=layers, taps=taps, split=split
    )
    out_cols = width - 2 * PAD
    done_rows = sum(total_rows - 2 * k for k in range(1, 2 * layers + 1))
    flops = 2 * levels * done_rows * out_cols * chans * chans * taps
    out = jax.ShapeDtypeStruct((levels, rows, chans, cols), jnp.bfloat16)
    buf = pltpu.VMEM((levels, total_rows, width, chans), jnp.float32)
    return pl.pallas_call(
        kernel,
        out_shape=(out, out),
        in_specs=[pl.BlockSpec(memory_space=pltpu.VMEM)] * 2,
        out_specs=(pl.BlockSpec(memory_space=pltpu.VMEM), pl.BlockSpec(memory_space=pltpu.VMEM)),
        scratch_shapes=[
            buf,
            pltpu.VMEM((levels, total_rows, width, lanes - chans), jnp.float32),
            buf,
            buf,
            buf,
            pltpu.VMEM((total_rows, out_cols, chans), jnp.float32),
            pltpu.VMEM((total_rows, width, chans), jnp.float32),
        ],
        cost_estimate=pl.CostEstimate(
            flops=flops, bytes_accessed=blk.size * 2 + 2 * levels * rows * cols * chans * 2, transcendentals=0
        ),
    )(blk, both)


def local(field, weights, coefs, land_mask, fold_flag):
    layers, taps = weights.shape[0], weights.shape[1]
    levels, rows, channels, cols = field.shape
    fold_sign = jnp.where(fold_flag == 1, -1.0, 1.0).astype(jnp.bfloat16)
    coef_stack = (
        coefs.reshape(layers, levels, rows, taps, cols)
        .transpose(1, 2, 0, 3, 4)
        .reshape(levels, rows, layers * taps, cols)
    )
    mask_stack = land_mask.astype(jnp.bfloat16)[:, :, None, :]
    block_in = jnp.concatenate([field, coef_stack, mask_stack], axis=2)
    block = block_in.transpose(0, 1, 3, 2)
    ext = exchange(block, block_in, fold_sign, taps, layers, channels)

    is_top = lax.axis_index("lat") == lax.axis_size("lat") - 1
    flipped = weights[:, ::-1] * fold_sign[None, None, :, None] * fold_sign[None, None, None, :]
    weights_high = jnp.where(is_top, flipped, weights)
    both = jnp.stack([weights, weights_high], axis=1)

    return run_model(ext, both, rows, cols, layers, taps, HALO + rows)


def solution(mesh):
    return jax.shard_map(
        local,
        mesh=mesh,
        in_specs=(
            P(None, "lat", None, "lon"),
            P(),
            P(None, "lat", None, "lon"),
            P(None, "lat", "lon"),
            P(),
        ),
        out_specs=(P(None, "lat", None, "lon"), P(None, "lat", None, "lon")),
        check_vma=False,
    )
```

```python
import functools

import jax
import jax.numpy as jnp
from jax import lax
from jax.experimental import pallas as pl
from jax.experimental.pallas import tpu as pltpu
from jax.sharding import PartitionSpec as P

HALO = 4
PAD = 8


def exchange(block, block_in, fold_sign, taps, layers, channels):
    rows = block.shape[1]
    cols = block.shape[2]
    nlon = lax.axis_size("lon")
    nlat = lax.axis_size("lat")
    to_right = [(i, (i + 1) % nlon) for i in range(nlon)]
    to_left = [((i + 1) % nlon, i) for i in range(nlon)]
    from_left = lax.ppermute(block[:, :, cols - HALO :], "lon", to_right)
    from_right = lax.ppermute(block[:, :, :HALO], "lon", to_left)

    top = nlat - 1
    top_rows = block[:, rows - HALO :]

    def across(piece, shift):
        pairs = [(b * nlat + top, ((shift - b) % nlon) * nlat + top) for b in range(nlon)]
        return lax.ppermute(piece, ("lon", "lat"), pairs)

    mirror_low = across(top_rows[:, :, cols - HALO :], nlon - 2)
    mirror_mid = across(block_in[:, rows - HALO :], nlon - 1).transpose(0, 1, 3, 2)
    mirror_high = across(top_rows[:, :, :HALO], nlon)
    mirrored = jnp.concatenate([mirror_low, mirror_mid, mirror_high], axis=2)
    wide = jnp.concatenate([from_left, block, from_right], axis=2)

    to_up = [(j, j + 1) for j in range(nlat - 1)]
    to_down = [(j + 1, j) for j in range(nlat - 1)]
    below = lax.ppermute(wide[:, rows - HALO :], "lat", to_up)
    above = lax.ppermute(wide[:, :HALO], "lat", to_down)
    mirrored = mirrored[:, ::-1, ::-1]
    field_part = mirrored[..., :channels] * fold_sign
    coef_part = mirrored[..., channels : channels + layers * taps]
    coef_part = coef_part.reshape(coef_part.shape[:3] + (layers, taps))[..., ::-1].reshape(
        coef_part.shape
    )
    rest = mirrored[..., channels + layers * taps :]
    mirrored = jnp.concatenate([field_part, coef_part, rest], axis=3)
    is_top = lax.axis_index("lat") == top
    above = jnp.where(is_top, mirrored, above)
    return jnp.concatenate([below, wide, above], axis=1)


def apply_layer(x_ref, aux_ref, w_ref, o_ref, acc_ref, lev, row_lo, row_hi, coef_lane, mask_lane, split, adjoint, mg_ref=None):
    out_cols = acc_ref.shape[1]
    chans = acc_ref.shape[2]
    acc_ref[...] = jnp.zeros(acc_ref.shape, acc_ref.dtype)
    if adjoint:
        src_rows = slice(row_lo - 1, row_hi + 1)
        mg_ref[src_rows] = x_ref[lev, src_rows] * aux_ref[lev, src_rows, :, pl.ds(mask_lane, 1)]
    for tap in range(w_ref.shape[1]):
        dj, di = tap // 3 - 1, tap % 3 - 1
        step = -dj if adjoint else dj
        col = PAD - di if adjoint else PAD + di
        if adjoint:
            groups = ((row_lo, min(row_hi, split + dj), 0), (max(row_lo, split + dj), row_hi, 1))
        else:
            groups = ((row_lo, min(row_hi, split), 0), (max(row_lo, split), row_hi, 1))
        for lo, hi, sel in groups:
            if hi <= lo:
                continue
            count = hi - lo
            src = slice(lo + step, hi + step)
            if adjoint:
                xin = mg_ref[src, pl.ds(col, out_cols), :].reshape(count * out_cols, chans)
                cf = aux_ref[lev, src, pl.ds(col, out_cols), pl.ds(coef_lane + tap, 1)]
                prod = jnp.dot(
                    xin.astype(jnp.bfloat16), w_ref[sel, tap], preferred_element_type=jnp.float32
                )
            else:
                xin = x_ref[lev, src, pl.ds(col, out_cols), :].reshape(count * out_cols, chans)
                cf = aux_ref[lev, lo:hi, pl.ds(PAD, out_cols), pl.ds(coef_lane + tap, 1)]
                prod = lax.dot_general(
                    xin.astype(jnp.bfloat16),
                    w_ref[sel, tap],
                    (((1,), (1,)), ((), ())),
                    preferred_element_type=jnp.float32,
                )
            term = cf.reshape(count * out_cols, 1) * prod
            acc_ref[lo:hi] += term.reshape(count, out_cols, chans)
    result = acc_ref[row_lo:row_hi]
    if not adjoint:
        result = result * aux_ref[lev, row_lo:row_hi, pl.ds(PAD, out_cols), pl.ds(mask_lane, 1)]
    o_ref[lev, row_lo:row_hi, pl.ds(PAD, out_cols), :] = result.astype(jnp.bfloat16).astype(jnp.float32)


def model_kernel(blk_ref, w_ref, fwd_ref, adj_ref, ext_ref, aux_ref, x1_ref, x2_ref, g1_ref, acc_ref, mg_ref, *, rows, cols, layers, taps, split):
    levels, total_rows = ext_ref.shape[0], ext_ref.shape[1]
    chans = ext_ref.shape[3]
    data_cols = blk_ref.shape[2]
    mask_lane = layers * taps
    for buf in (ext_ref, aux_ref, x1_ref, x2_ref, g1_ref):
        edge = buf.shape[:2] + (PAD, buf.shape[3])
        buf[:, :, pl.ds(0, PAD), :] = jnp.zeros(edge, buf.dtype)
        buf[:, :, pl.ds(buf.shape[2] - PAD, PAD), :] = jnp.zeros(edge, buf.dtype)
    for lev in range(levels):
        for j in range(total_rows):
            piece = blk_ref[lev, j].astype(jnp.float32)
            ext_ref[lev, j, pl.ds(PAD, data_cols), :] = piece[:, :chans]
            aux_ref[lev, j, pl.ds(PAD, data_cols), :] = piece[:, chans:]

    def store_transposed(out_ref, src_ref, lev):
        for r in range(rows):
            tile = src_ref[lev, HALO + r, pl.ds(PAD + HALO, cols), :]
            out_ref[lev, r] = jnp.transpose(tile).astype(out_ref.dtype)

    def level_body(lev, carry):
        apply_layer(ext_ref, aux_ref, w_ref.at[0], x1_ref, acc_ref, lev, 1, total_rows - 1, 0, mask_lane, split, False)
        apply_layer(x1_ref, aux_ref, w_ref.at[1], x2_ref, acc_ref, lev, 2, total_rows - 2, taps, mask_lane, split, False)
        store_transposed(fwd_ref, x2_ref, lev)
        apply_layer(x2_ref, aux_ref, w_ref.at[1], g1_ref, acc_ref, lev, 3, total_rows - 3, taps, mask_lane, split, True, mg_ref)
        apply_layer(g1_ref, aux_ref, w_ref.at[0], x1_ref, acc_ref, lev, 4, total_rows - 4, 0, mask_lane, split, True, mg_ref)
        store_transposed(adj_ref, x1_ref, lev)
        return carry

    lax.fori_loop(0, levels, level_body, 0)


def run_model(blk, both, rows, cols, layers, taps, split):
    levels, total_rows, data_cols, lanes = blk.shape
    chans = both.shape[-1]
    width = data_cols + 2 * PAD
    kernel = functools.partial(
        model_kernel, rows=rows, cols=cols, layers=layers, taps=taps, split=split
    )
    out_cols = width - 2 * PAD
    done_rows = sum(total_rows - 2 * k for k in range(1, 2 * layers + 1))
    flops = 2 * levels * done_rows * out_cols * chans * chans * taps
    out = jax.ShapeDtypeStruct((levels, rows, chans, cols), jnp.bfloat16)
    buf = pltpu.VMEM((levels, total_rows, width, chans), jnp.float32)
    return pl.pallas_call(
        kernel,
        out_shape=(out, out),
        in_specs=[pl.BlockSpec(memory_space=pltpu.VMEM)] * 2,
        out_specs=(pl.BlockSpec(memory_space=pltpu.VMEM), pl.BlockSpec(memory_space=pltpu.VMEM)),
        scratch_shapes=[
            buf,
            pltpu.VMEM((levels, total_rows, width, lanes - chans), jnp.float32),
            buf,
            buf,
            buf,
            pltpu.VMEM((total_rows, out_cols, chans), jnp.float32),
            pltpu.VMEM((total_rows, width, chans), jnp.float32),
        ],
        cost_estimate=pl.CostEstimate(
            flops=flops, bytes_accessed=blk.size * 2 + 2 * levels * rows * cols * chans * 2, transcendentals=0
        ),
    )(blk, both)


def local(field, weights, coefs, land_mask, fold_flag):
    layers, taps = weights.shape[0], weights.shape[1]
    levels, rows, channels, cols = field.shape
    fold_sign = jnp.where(fold_flag == 1, -1.0, 1.0).astype(jnp.bfloat16)
    coef_stack = (
        coefs.reshape(layers, levels, rows, taps, cols)
        .transpose(1, 2, 0, 3, 4)
        .reshape(levels, rows, layers * taps, cols)
    )
    mask_stack = land_mask.astype(jnp.bfloat16)[:, :, None, :]
    block_in = jnp.concatenate([field, coef_stack, mask_stack], axis=2)
    block = block_in.transpose(0, 1, 3, 2)
    ext = exchange(block, block_in, fold_sign, taps, layers, channels)

    is_top = lax.axis_index("lat") == lax.axis_size("lat") - 1
    flipped = weights[:, ::-1] * fold_sign[None, None, :, None] * fold_sign[None, None, None, :]
    weights_high = jnp.where(is_top, flipped, weights)
    both = jnp.stack([weights, weights_high], axis=1)

    return run_model(ext, both, rows, cols, layers, taps, HALO + rows)


def solution(mesh):
    return jax.shard_map(
        local,
        mesh=mesh,
        in_specs=(
            P(None, "lat", None, "lon"),
            P(),
            P(None, "lat", None, "lon"),
            P(None, "lat", "lon"),
            P(),
        ),
        out_specs=(P(None, "lat", None, "lon"), P(None, "lat", None, "lon")),
        check_vma=False,
    )
```
